32 devices in a mesh: var: 8 (over z, y), samp: 4 (over x, core).
Axes of the slice: x: 2, y: 2, z: 4, core: 2. Of those that a mesh axis runs over, the one named last changes fastest.
Arguments:
- dosages: bfloat16 [8192, 6144], P('samp', 'var'), may hold values from 0 to 2
- observed: int32 [8192, 6144], P('samp', 'var'), may hold values 0 or 1
Outputs:
- ld_scores: float32 [6144], P(('var', 'samp'))
The draws below stay inside these ranges and needn't reach their ends.
All inputs are finite; a program needn't handle non-finite values. No bound on the sum of `observed` on one device may be relied on, other than what follows from the above.
Results may differ from the reference program's by a relative error of at most 0.00055.
Values may be sent and summed in bfloat16 or wider, within the bound.
No kernel may reach another device: no remote copies, remote signals or barrier semaphores. Data moves between devices by JAX's collectives and lax.ppermute only.
A program may use at most 192 MiB of HBM per device.

```python
import jax
import jax.numpy as jnp
from jax import lax

BLK = 768
BAND = 3
SAMPLES = 8192
VARIANTS = 6144


def draw_dosages(key, part):
    subkeys = jax.random.split(key, 12)
    positions = jnp.arange(VARIANTS)
    latent = jax.random.normal(subkeys[0], (SAMPLES, VARIANTS), jnp.float32)
    for level, seg_len in enumerate((BLK // 2, 2 * BLK, 4 * BLK)):
        offset = jax.random.randint(subkeys[1 + level], (), 0, seg_len)
        seg_count = VARIANTS // seg_len + 2
        factor = jax.random.normal(subkeys[4 + level], (SAMPLES, seg_count), jnp.float32)
        loading = jnp.exp(jax.random.uniform(subkeys[7 + level], (VARIANTS,), jnp.float32, -1.0, 0.5))
        latent = latent + factor[:, (positions + offset) // seg_len] * loading
    center = jax.random.uniform(subkeys[11], (VARIANTS,), jnp.float32, -1.5, 1.5)
    return (2.0 * jax.nn.sigmoid(0.6 * latent + center)).astype(jnp.bfloat16)


def touch_ends(entries, key, low, high):
    longest = entries.shape.index(max(entries.shape))
    spots = []
    for shift in (0, 1):
        where = [jax.random.randint(jax.random.fold_in(key, axis), (), 0, length) for axis, length in enumerate(entries.shape)]
        where[longest] = (where[longest] + shift) % entries.shape[longest]
        spots.append(tuple(where))
    return entries.at[spots[0]].set(low).at[spots[1]].set(high)


def setup_inputs(seed: int = 0) -> dict:
    seeds = jax.random.split(jax.random.key(seed), 3)
    return {
        "dosages": draw_dosages(jax.random.fold_in(seeds[2], 71), 0),
        "observed": touch_ends((jax.random.randint(seeds[1], (SAMPLES, VARIANTS), 0, 10) < 9).astype(jnp.int32), jax.random.fold_in(seeds[1], 1), 0, 1),
    }


def standardize(dose_block, mask_block):
    values = dose_block.astype(jnp.float32)
    present = mask_block.astype(jnp.float32)
    seen_count = jnp.maximum(lax.optimization_barrier(jnp.sum(present, 0)), 1.0)
    column_mean = lax.optimization_barrier(jnp.sum(present * values, 0)) / seen_count
    spread = lax.optimization_barrier(jnp.sum(present * values * values, 0)) / seen_count - column_mean * column_mean
    return ((values - column_mean) * lax.rsqrt(spread + 1e-05) * present).astype(jnp.bfloat16)

def adjusted_r2(gram_part):
    correl = gram_part / SAMPLES
    squared = correl * correl
    return squared - (1.0 - squared) / (SAMPLES - 2)

def reference(dosages, observed):
    block_count = VARIANTS // BLK
    dosage_blocks = dosages.reshape(SAMPLES, block_count, BLK).transpose(1, 0, 2)
    mask_blocks = observed.reshape(SAMPLES, block_count, BLK).transpose(1, 0, 2)
    standard = lax.map(lambda pair_in: standardize(pair_in[0], pair_in[1]), (dosage_blocks, mask_blocks))
    padded = jnp.concatenate([standard, jnp.zeros((BAND, SAMPLES, BLK), jnp.bfloat16)], 0)

    def one_block(block_id):
        own_block = lax.dynamic_index_in_dim(standard, block_id, 0, keepdims=False)
        row_sums = jnp.zeros((BLK,), jnp.float32)
        col_list = []
        for offset in range(BAND + 1):
            partner = lax.dynamic_index_in_dim(padded, block_id + offset, 0, keepdims=False)
            gram_part = lax.dot_general(own_block, partner, (((0,), (0,)), ((), ())), preferred_element_type=jnp.float32)
            in_range = (block_id + offset < block_count).astype(jnp.float32)
            adjusted = adjusted_r2(gram_part) * in_range
            row_sums = row_sums + lax.optimization_barrier(jnp.sum(adjusted, 1))
            if offset > 0:
                col_list.append(lax.optimization_barrier(jnp.sum(adjusted, 0)))
        return (row_sums, jnp.stack(col_list))
    row_sums, col_sums = lax.map(one_block, jnp.arange(block_count, dtype=jnp.int32))
    col_padded = jnp.concatenate([jnp.zeros((BAND, BAND, BLK), jnp.float32), col_sums], 0)
    ld_total = row_sums
    for offset in range(1, BAND + 1):
        ld_total = ld_total + col_padded[BAND - offset:BAND - offset + block_count, offset - 1]
    return (ld_total / BLK).reshape(VARIANTS)
```

```python
import jax
import jax.numpy as jnp
from jax import lax
from jax.sharding import PartitionSpec as P

BAND = 3
PARTNER_STEP = {1: 1, 2: 2, 3: -3}


def from_behind(value, axis, steps):
    count = lax.axis_size(axis)
    leading, last = (max(0, -steps), min(count, count - steps))
    return lax.ppermute(value, axis, [(source, source + steps) for source in range(leading, last)])


def adjusted_r2(gram_part, samples):
    correl = gram_part / samples
    squared = correl * correl
    return squared - (1.0 - squared) / (samples - 2)


def gram_of(left, right):
    return lax.dot_general(left, right, (((0,), (0,)), ((), ())), preferred_element_type=jnp.float32)


def reduce_to_owner(part, owner, n_samp):
    pairs_core = [(s, s ^ 1) for s in range(n_samp) if (s & 1) != (owner & 1)]
    summed = part + lax.ppermute(part.astype(jnp.bfloat16), "samp", pairs_core).astype(jnp.float32)
    pairs_chip = [(owner ^ 2, owner)]
    return summed + lax.ppermute(summed.astype(jnp.bfloat16), "samp", pairs_chip).astype(jnp.float32)


def local(dosages, observed):
    values = dosages.astype(jnp.float32)
    present = observed.astype(jnp.float32)
    seen_count, first_sum, second_sum = lax.psum(
        (jnp.sum(present, 0), jnp.sum(present * values, 0), jnp.sum(present * values * values, 0)),
        "samp",
    )
    seen_count = jnp.maximum(seen_count, 1.0)
    column_mean = first_sum / seen_count
    spread = second_sum / seen_count - column_mean * column_mean
    standard = ((values - column_mean) * lax.rsqrt(spread + 1e-05) * present).astype(jnp.bfloat16)
    n_samp = lax.axis_size("samp")
    n_var = lax.axis_size("var")
    samples = standard.shape[0] * n_samp
    block_width = standard.shape[1]
    position = lax.axis_index("var")
    me = lax.axis_index("samp")

    owned = [reduce_to_owner(gram_of(standard, standard), 0, n_samp)]
    for offset in range(1, BAND + 1):
        step = PARTNER_STEP[offset]
        partner = from_behind(standard, "var", -step)
        owned.append(reduce_to_owner(gram_of(standard, partner), offset, n_samp))
    gram = lax.dynamic_index_in_dim(jnp.stack(owned), me, 0, keepdims=False)

    steps = jnp.array([0] + [PARTNER_STEP[d] for d in range(1, BAND + 1)], jnp.int32)
    target = position + steps[me]
    in_range = ((target >= 0) & (target < n_var)).astype(jnp.float32)
    adjusted = adjusted_r2(gram, samples) * in_range
    row_sums = jnp.sum(adjusted, 1)
    col_sums = jnp.sum(adjusted, 0) * (me > 0).astype(jnp.float32)
    pairs = []
    for var_idx in range(n_var):
        for offset in range(1, BAND + 1):
            dest = var_idx + PARTNER_STEP[offset]
            if 0 <= dest < n_var:
                pairs.append((var_idx * n_samp + offset, dest * n_samp + offset))
    moved = lax.ppermute(col_sums, ("var", "samp"), pairs)
    total = lax.psum_scatter(row_sums + moved, "samp", scatter_dimension=0, tiled=True)
    return total / block_width


def solution(mesh):
    placed = (P("samp", "var"), P("samp", "var"))
    return jax.shard_map(
        local, mesh=mesh, in_specs=placed, out_specs=P(("var", "samp")), check_vma=False
    )
```

```python
import jax
import jax.numpy as jnp
from jax import lax
from jax.sharding import PartitionSpec as P

BAND = 3
PARTNER_STEP = {1: 1, 2: 2, 3: -3}
PROCESS_ORDER = (2, 3, 1)


def from_behind(value, axis, steps):
    count = lax.axis_size(axis)
    leading, last = (max(0, -steps), min(count, count - steps))
    return lax.ppermute(value, axis, [(source, source + steps) for source in range(leading, last)])


def adjusted_r2(gram_part, samples):
    correl = gram_part / samples
    squared = correl * correl
    return squared - (1.0 - squared) / (samples - 2)


def gram_of(left, right):
    return lax.dot_general(left, right, (((0,), (0,)), ((), ())), preferred_element_type=jnp.float32)


def reduce_to_owner(part, owner, n_samp):
    pairs_core = [(s, s ^ 1) for s in range(n_samp) if (s & 1) != (owner & 1)]
    summed = part + lax.ppermute(part.astype(jnp.bfloat16), "samp", pairs_core).astype(jnp.float32)
    pairs_chip = [(owner ^ 2, owner)]
    return summed + lax.ppermute(summed.astype(jnp.bfloat16), "samp", pairs_chip).astype(jnp.float32)


def local(dosages, observed):
    coded = jnp.where(observed != 0, dosages, jnp.asarray(-1, dosages.dtype))
    raw = {offset: from_behind(coded, "var", -PARTNER_STEP[offset]) for offset in range(1, BAND + 1)}
    values = dosages.astype(jnp.float32)
    present = observed.astype(jnp.float32)
    seen_count, first_sum, second_sum = lax.psum(
        (jnp.sum(present, 0), jnp.sum(present * values, 0), jnp.sum(present * values * values, 0)),
        "samp",
    )
    seen_count = jnp.maximum(seen_count, 1.0)
    column_mean = first_sum / seen_count
    spread = second_sum / seen_count - column_mean * column_mean
    inverse_sd = lax.rsqrt(spread + 1e-05)
    standard = ((values - column_mean) * inverse_sd * present).astype(jnp.bfloat16)
    scales = jnp.stack([column_mean, inverse_sd])
    n_samp = lax.axis_size("samp")
    n_var = lax.axis_size("var")
    samples = standard.shape[0] * n_samp
    block_width = standard.shape[1]
    position = lax.axis_index("var")
    me = lax.axis_index("samp")

    owned = {0: reduce_to_owner(gram_of(standard, standard), 0, n_samp)}
    done = owned[0]
    for offset in PROCESS_ORDER:
        partner_scales = from_behind(scales, "var", -PARTNER_STEP[offset])
        coded_partner, partner_scales, done = lax.optimization_barrier((raw[offset], partner_scales, done))
        partner_values = coded_partner.astype(jnp.float32)
        partner_present = (partner_values >= 0).astype(jnp.float32)
        partner = ((partner_values - partner_scales[0]) * partner_scales[1] * partner_present).astype(jnp.bfloat16)
        owned[offset] = reduce_to_owner(gram_of(standard, partner), offset, n_samp)
        done = owned[offset]
    gram = lax.dynamic_index_in_dim(jnp.stack([owned[d] for d in range(BAND + 1)]), me, 0, keepdims=False)

    steps = jnp.array([0] + [PARTNER_STEP[d] for d in range(1, BAND + 1)], jnp.int32)
    target = position + steps[me]
    in_range = ((target >= 0) & (target < n_var)).astype(jnp.float32)
    adjusted = adjusted_r2(gram, samples) * in_range
    row_sums = jnp.sum(adjusted, 1)
    col_sums = jnp.sum(adjusted, 0) * (me > 0).astype(jnp.float32)
    pairs = []
    for var_idx in range(n_var):
        for offset in range(1, BAND + 1):
            dest = var_idx + PARTNER_STEP[offset]
            if 0 <= dest < n_var:
                pairs.append((var_idx * n_samp + offset, dest * n_samp + offset))
    moved = lax.ppermute(col_sums, ("var", "samp"), pairs)
    total = lax.psum_scatter(row_sums + moved, "samp", scatter_dimension=0, tiled=True)
    return total / block_width


def solution(mesh):
    placed = (P("samp", "var"), P("samp", "var"))
    return jax.shard_map(
        local, mesh=mesh, in_specs=placed, out_specs=P(("var", "samp")), check_vma=False
    )
```

```python
import jax
import jax.numpy as jnp
from jax import lax
from jax.sharding import PartitionSpec as P

BAND = 3
PARTNER_STEP = {1: 1, 2: 2, 3: -3}
PROCESS_ORDER = (2, 3, 1)


def from_behind(value, axis, steps):
    count = lax.axis_size(axis)
    leading, last = (max(0, -steps), min(count, count - steps))
    return lax.ppermute(value, axis, [(source, source + steps) for source in range(leading, last)])


def adjusted_r2(gram_part, samples):
    correl = gram_part / samples
    squared = correl * correl
    return squared - (1.0 - squared) / (samples - 2)


def gram_of(left, right):
    return lax.dot_general(left, right, (((0,), (0,)), ((), ())), preferred_element_type=jnp.float32)


def reduce_to_owner(part, owner, n_samp):
    pairs_core = [(s, s ^ 1) for s in range(n_samp) if (s & 1) != (owner & 1)]
    summed = part + lax.ppermute(part.astype(jnp.bfloat16), "samp", pairs_core).astype(jnp.float32)
    pairs_chip = [(owner ^ 2, owner)]
    return summed + lax.ppermute(summed.astype(jnp.bfloat16), "samp", pairs_chip).astype(jnp.float32)


def local(dosages, observed):
    coded = jnp.where(observed != 0, dosages, jnp.asarray(-1, dosages.dtype))
    raw = {offset: from_behind(coded, "var", -PARTNER_STEP[offset]) for offset in range(1, BAND + 1)}
    values = dosages.astype(jnp.float32)
    present = observed.astype(jnp.float32)
    n_samp = lax.axis_size("samp")
    n_var = lax.axis_size("var")
    position = lax.axis_index("var")
    me = lax.axis_index("samp")
    partial = jnp.stack([jnp.sum(present, 0), jnp.sum(present * values, 0), jnp.sum(present * values * values, 0)])
    slots = jnp.zeros((n_var,) + partial.shape, jnp.float32)
    stats = lax.psum(lax.dynamic_update_index_in_dim(slots, partial, position, 0), ("var", "samp"))
    seen_count = jnp.maximum(stats[:, 0], 1.0)
    column_mean = stats[:, 1] / seen_count
    spread = stats[:, 2] / seen_count - column_mean * column_mean
    inverse_sd = lax.rsqrt(spread + 1e-05)
    own_mean = lax.dynamic_index_in_dim(column_mean, position, 0, keepdims=False)
    own_sd = lax.dynamic_index_in_dim(inverse_sd, position, 0, keepdims=False)
    standard = ((values - own_mean) * own_sd * present).astype(jnp.bfloat16)
    samples = standard.shape[0] * n_samp
    block_width = standard.shape[1]

    owned = {0: reduce_to_owner(gram_of(standard, standard), 0, n_samp)}
    arrived, owned[0] = lax.optimization_barrier(([raw[d] for d in PROCESS_ORDER], owned[0]))
    for offset, coded_partner in zip(PROCESS_ORDER, arrived):
        source = jnp.clip(position + PARTNER_STEP[offset], 0, n_var - 1)
        partner_mean = lax.dynamic_index_in_dim(column_mean, source, 0, keepdims=False)
        partner_sd = lax.dynamic_index_in_dim(inverse_sd, source, 0, keepdims=False)
        partner_values = coded_partner.astype(jnp.float32)
        partner_present = (partner_values >= 0).astype(jnp.float32)
        partner = ((partner_values - partner_mean) * partner_sd * partner_present).astype(jnp.bfloat16)
        owned[offset] = reduce_to_owner(gram_of(standard, partner), offset, n_samp)
    gram = lax.dynamic_index_in_dim(jnp.stack([owned[d] for d in range(BAND + 1)]), me, 0, keepdims=False)

    steps = jnp.array([0] + [PARTNER_STEP[d] for d in range(1, BAND + 1)], jnp.int32)
    target = position + steps[me]
    in_range = ((target >= 0) & (target < n_var)).astype(jnp.float32)
    adjusted = adjusted_r2(gram, samples) * in_range
    row_sums = jnp.sum(adjusted, 1)
    col_sums = jnp.sum(adjusted, 0) * (me > 0).astype(jnp.float32)
    pairs = []
    for var_idx in range(n_var):
        for offset in range(1, BAND + 1):
            dest = var_idx + PARTNER_STEP[offset]
            if 0 <= dest < n_var:
                pairs.append((var_idx * n_samp + offset, dest * n_samp + offset))
    moved = lax.ppermute(col_sums, ("var", "samp"), pairs)
    total = lax.psum_scatter(row_sums + moved, "samp", scatter_dimension=0, tiled=True)
    return total / block_width


def solution(mesh):
    placed = (P("samp", "var"), P("samp", "var"))
    return jax.shard_map(
        local, mesh=mesh, in_specs=placed, out_specs=P(("var", "samp")), check_vma=False
    )
```

```python
import jax
import jax.numpy as jnp
from jax import lax
from jax.sharding import PartitionSpec as P

BAND = 3
PARTNER_STEP = {1: 1, 2: 2, 3: -3}
PROCESS_ORDER = (2, 3, 1)


def from_behind(value, axis, steps):
    count = lax.axis_size(axis)
    leading, last = (max(0, -steps), min(count, count - steps))
    return lax.ppermute(value, axis, [(source, source + steps) for source in range(leading, last)])


def adjusted_r2(gram_part, samples):
    correl = gram_part / samples
    squared = correl * correl
    return squared - (1.0 - squared) / (samples - 2)


def gram_of(left, right):
    return lax.dot_general(left, right, (((0,), (0,)), ((), ())), preferred_element_type=jnp.float32)


def reduce_to_owner(part, owner, n_samp):
    pairs_core = [(s, s ^ 1) for s in range(n_samp) if (s & 1) != (owner & 1)]
    summed = part + lax.ppermute(part.astype(jnp.bfloat16), "samp", pairs_core).astype(jnp.float32)
    pairs_chip = [(owner ^ 2, owner)]
    return summed + lax.ppermute(summed.astype(jnp.bfloat16), "samp", pairs_chip).astype(jnp.float32)


def local(dosages, observed):
    coded = jnp.where(observed != 0, dosages, jnp.asarray(-1, dosages.dtype))
    raw = {offset: from_behind(coded, "var", -PARTNER_STEP[offset]) for offset in range(1, BAND + 1)}
    values = dosages.astype(jnp.float32)
    present = observed.astype(jnp.float32)
    n_samp = lax.axis_size("samp")
    n_var = lax.axis_size("var")
    position = lax.axis_index("var")
    me = lax.axis_index("samp")
    partial = jnp.stack([jnp.sum(present, 0), jnp.sum(present * values, 0), jnp.sum(present * values * values, 0)])
    stats = lax.all_gather(lax.psum(partial, "samp"), "var")
    seen_count = jnp.maximum(stats[:, 0], 1.0)
    column_mean = stats[:, 1] / seen_count
    spread = stats[:, 2] / seen_count - column_mean * column_mean
    inverse_sd = lax.rsqrt(spread + 1e-05)
    own_mean = lax.dynamic_index_in_dim(column_mean, position, 0, keepdims=False)
    own_sd = lax.dynamic_index_in_dim(inverse_sd, position, 0, keepdims=False)
    standard = ((values - own_mean) * own_sd * present).astype(jnp.bfloat16)
    samples = standard.shape[0] * n_samp
    block_width = standard.shape[1]

    owned = {0: reduce_to_owner(gram_of(standard, standard), 0, n_samp)}
    arrived, owned[0] = lax.optimization_barrier(([raw[d] for d in PROCESS_ORDER], owned[0]))
    for offset, coded_partner in zip(PROCESS_ORDER, arrived):
        source = jnp.clip(position + PARTNER_STEP[offset], 0, n_var - 1)
        partner_mean = lax.dynamic_index_in_dim(column_mean, source, 0, keepdims=False)
        partner_sd = lax.dynamic_index_in_dim(inverse_sd, source, 0, keepdims=False)
        partner_values = coded_partner.astype(jnp.float32)
        partner_present = (partner_values >= 0).astype(jnp.float32)
        partner = ((partner_values - partner_mean) * partner_sd * partner_present).astype(jnp.bfloat16)
        owned[offset] = reduce_to_owner(gram_of(standard, partner), offset, n_samp)
    gram = lax.dynamic_index_in_dim(jnp.stack([owned[d] for d in range(BAND + 1)]), me, 0, keepdims=False)

    steps = jnp.array([0] + [PARTNER_STEP[d] for d in range(1, BAND + 1)], jnp.int32)
    target = position + steps[me]
    in_range = ((target >= 0) & (target < n_var)).astype(jnp.float32)
    adjusted = adjusted_r2(gram, samples) * in_range
    row_sums = jnp.sum(adjusted, 1)
    col_sums = jnp.sum(adjusted, 0) * (me > 0).astype(jnp.float32)
    pairs = []
    for var_idx in range(n_var):
        for offset in range(1, BAND + 1):
            dest = var_idx + PARTNER_STEP[offset]
            if 0 <= dest < n_var:
                pairs.append((var_idx * n_samp + offset, dest * n_samp + offset))
    moved = lax.ppermute(col_sums, ("var", "samp"), pairs)
    total = lax.psum_scatter(row_sums + moved, "samp", scatter_dimension=0, tiled=True)
    return total / block_width


def solution(mesh):
    placed = (P("samp", "var"), P("samp", "var"))
    return jax.shard_map(
        local, mesh=mesh, in_specs=placed, out_specs=P(("var", "samp")), check_vma=False
    )
```

```python
import jax
import jax.numpy as jnp
from jax import lax
from jax.sharding import PartitionSpec as P

BAND = 3
PARTNER_STEP = {1: 1, 2: 2, 3: -3}
PROCESS_ORDER = (2, 3, 1)


def from_behind(value, axis, steps):
    count = lax.axis_size(axis)
    leading, last = (max(0, -steps), min(count, count - steps))
    return lax.ppermute(value, axis, [(source, source + steps) for source in range(leading, last)])


def adjusted_r2(gram_part, samples):
    correl = gram_part / samples
    squared = correl * correl
    return squared - (1.0 - squared) / (samples - 2)


def gram_of(left, right):
    return lax.dot_general(left, right, (((0,), (0,)), ((), ())), preferred_element_type=jnp.float32)


def reduce_to_owner(part, owner, n_samp):
    pairs_core = [(s, s ^ 1) for s in range(n_samp) if (s & 1) != (owner & 1)]
    summed = part + lax.ppermute(part.astype(jnp.bfloat16), "samp", pairs_core).astype(jnp.float32)
    pairs_chip = [(owner ^ 2, owner)]
    return summed + lax.ppermute(summed.astype(jnp.bfloat16), "samp", pairs_chip).astype(jnp.float32)


def standardize(values, present, axis):
    seen_count, first_sum, second_sum = lax.psum(
        (jnp.sum(present, -2), jnp.sum(present * values, -2), jnp.sum(present * values * values, -2)),
        axis,
    )
    seen_count = jnp.maximum(seen_count, 1.0)
    column_mean = first_sum / seen_count
    spread = second_sum / seen_count - column_mean * column_mean
    scale = lax.rsqrt(spread + 1e-05)
    return ((values - column_mean[..., None, :]) * scale[..., None, :] * present).astype(jnp.bfloat16)


def local(dosages, observed):
    coded = jnp.where(observed != 0, dosages, jnp.asarray(-1, dosages.dtype))
    raw = {offset: from_behind(coded, "var", -PARTNER_STEP[offset]) for offset in range(1, BAND + 1)}
    values = dosages.astype(jnp.float32)
    present = observed.astype(jnp.float32)
    n_samp = lax.axis_size("samp")
    n_var = lax.axis_size("var")
    position = lax.axis_index("var")
    me = lax.axis_index("samp")
    standard = standardize(values, present, "samp")
    samples = standard.shape[0] * n_samp
    block_width = standard.shape[1]

    owned = {0: reduce_to_owner(gram_of(standard, standard), 0, n_samp)}
    arrived, owned[0] = lax.optimization_barrier(([raw[d] for d in PROCESS_ORDER], owned[0]))
    partner_values = jnp.stack([coded_partner.astype(jnp.float32) for coded_partner in arrived])
    partner_present = (partner_values >= 0).astype(jnp.float32)
    partners = standardize(partner_values, partner_present, "samp")
    for index, offset in enumerate(PROCESS_ORDER):
        owned[offset] = reduce_to_owner(gram_of(standard, partners[index]), offset, n_samp)
    gram = lax.dynamic_index_in_dim(jnp.stack([owned[d] for d in range(BAND + 1)]), me, 0, keepdims=False)

    steps = jnp.array([0] + [PARTNER_STEP[d] for d in range(1, BAND + 1)], jnp.int32)
    target = position + steps[me]
    in_range = ((target >= 0) & (target < n_var)).astype(jnp.float32)
    adjusted = adjusted_r2(gram, samples) * in_range
    row_sums = jnp.sum(adjusted, 1)
    col_sums = jnp.sum(adjusted, 0) * (me > 0).astype(jnp.float32)
    pairs = []
    for var_idx in range(n_var):
        for offset in range(1, BAND + 1):
            dest = var_idx + PARTNER_STEP[offset]
            if 0 <= dest < n_var:
                pairs.append((var_idx * n_samp + offset, dest * n_samp + offset))
    moved = lax.ppermute(col_sums, ("var", "samp"), pairs)
    total = lax.psum_scatter(row_sums + moved, "samp", scatter_dimension=0, tiled=True)
    return total / block_width


def solution(mesh):
    placed = (P("samp", "var"), P("samp", "var"))
    return jax.shard_map(
        local, mesh=mesh, in_specs=placed, out_specs=P(("var", "samp")), check_vma=False
    )
```

```python
import jax
import jax.numpy as jnp
from jax import lax
from jax.sharding import PartitionSpec as P

BAND = 3
PARTNER_STEP = {1: 1, 2: 2, 3: -3}
PROCESS_ORDER = (2, 3, 1)


def from_behind(value, axis, steps):
    count = lax.axis_size(axis)
    leading, last = (max(0, -steps), min(count, count - steps))
    return lax.ppermute(value, axis, [(source, source + steps) for source in range(leading, last)])


def adjusted_r2(gram_part, samples):
    correl = gram_part / samples
    squared = correl * correl
    return squared - (1.0 - squared) / (samples - 2)


def gram_of(left, right):
    return lax.dot_general(left, right, (((0,), (0,)), ((), ())), preferred_element_type=jnp.float32)


def reduce_quarters(part, n_samp):
    me = lax.axis_index("samp")
    core, chip = me % 2, me // 2
    quarters = part.reshape(2, 2, part.shape[0] // 4, part.shape[1])
    keep = lax.dynamic_index_in_dim(quarters, core, 1, keepdims=False)
    send = lax.dynamic_index_in_dim(quarters, 1 - core, 1, keepdims=False)
    pairs_core = [(s, s ^ 1) for s in range(n_samp)]
    summed = keep + lax.ppermute(send.astype(jnp.bfloat16), "samp", pairs_core).astype(jnp.float32)
    keep = lax.dynamic_index_in_dim(summed, chip, 0, keepdims=False)
    send = lax.dynamic_index_in_dim(summed, 1 - chip, 0, keepdims=False)
    pairs_chip = [(s, s ^ 2) for s in range(n_samp)]
    return keep + lax.ppermute(send.astype(jnp.bfloat16), "samp", pairs_chip).astype(jnp.float32)


def local(dosages, observed):
    values = dosages.astype(jnp.float32)
    present = observed.astype(jnp.float32)
    seen_count, first_sum, second_sum = lax.psum(
        (jnp.sum(present, 0), jnp.sum(present * values, 0), jnp.sum(present * values * values, 0)),
        "samp",
    )
    seen_count = jnp.maximum(seen_count, 1.0)
    column_mean = first_sum / seen_count
    spread = second_sum / seen_count - column_mean * column_mean
    standard = ((values - column_mean) * lax.rsqrt(spread + 1e-05) * present).astype(jnp.bfloat16)
    n_samp = lax.axis_size("samp")
    n_var = lax.axis_size("var")
    samples = standard.shape[0] * n_samp
    block_width = standard.shape[1]
    position = lax.axis_index("var")
    raw = {offset: from_behind(standard, "var", -PARTNER_STEP[offset]) for offset in range(1, BAND + 1)}

    owned = {0: reduce_quarters(gram_of(standard, standard), n_samp)}
    arrived, owned[0] = lax.optimization_barrier(([raw[d] for d in PROCESS_ORDER], owned[0]))
    for offset, partner in zip(PROCESS_ORDER, arrived):
        owned[offset] = reduce_quarters(gram_of(standard, partner), n_samp)

    row_total = jnp.sum(adjusted_r2(owned[0], samples), 1)
    incoming = jnp.zeros((block_width,), jnp.float32)
    for offset in range(1, BAND + 1):
        step = PARTNER_STEP[offset]
        in_range = ((position + step >= 0) & (position + step < n_var)).astype(jnp.float32)
        adjusted = adjusted_r2(owned[offset], samples) * in_range
        row_total = row_total + jnp.sum(adjusted, 1)
        incoming = incoming + from_behind(jnp.sum(adjusted, 0), "var", step)
    total = row_total + lax.psum_scatter(incoming, "samp", scatter_dimension=0, tiled=True)
    return total / block_width


def solution(mesh):
    placed = (P("samp", "var"), P("samp", "var"))
    return jax.shard_map(
        local, mesh=mesh, in_specs=placed, out_specs=P(("var", "samp")), check_vma=False
    )
```

```python
import jax
import jax.numpy as jnp
from jax import lax
from jax.sharding import PartitionSpec as P

BAND = 3
PARTNER_STEP = {1: 1, 2: 2, 3: -3}
PROCESS_ORDER = (2, 3, 1)


def from_behind(value, axis, steps):
    count = lax.axis_size(axis)
    leading, last = (max(0, -steps), min(count, count - steps))
    return lax.ppermute(value, axis, [(source, source + steps) for source in range(leading, last)])


def adjusted_r2(gram_part, samples):
    correl = gram_part / samples
    squared = correl * correl
    return squared - (1.0 - squared) / (samples - 2)


def gram_of(left, right):
    return lax.dot_general(left, right, (((0,), (0,)), ((), ())), preferred_element_type=jnp.float32)


def reduce_quarters(part, n_samp):
    me = lax.axis_index("samp")
    core, chip = me % 2, me // 2
    quarters = part.reshape(2, 2, part.shape[0] // 4, part.shape[1])
    keep = lax.dynamic_index_in_dim(quarters, core, 1, keepdims=False)
    send = lax.dynamic_index_in_dim(quarters, 1 - core, 1, keepdims=False)
    pairs_core = [(s, s ^ 1) for s in range(n_samp)]
    summed = keep + lax.ppermute(send.astype(jnp.bfloat16), "samp", pairs_core).astype(jnp.float32)
    keep = lax.dynamic_index_in_dim(summed, chip, 0, keepdims=False)
    send = lax.dynamic_index_in_dim(summed, 1 - chip, 0, keepdims=False)
    pairs_chip = [(s, s ^ 2) for s in range(n_samp)]
    return keep + lax.ppermute(send.astype(jnp.bfloat16), "samp", pairs_chip).astype(jnp.float32)


def local(dosages, observed):
    values = dosages.astype(jnp.float32)
    present = observed.astype(jnp.float32)
    seen_count, first_sum, second_sum = lax.psum(
        (jnp.sum(present, 0), jnp.sum(present * values, 0), jnp.sum(present * values * values, 0)),
        "samp",
    )
    seen_count = jnp.maximum(seen_count, 1.0)
    column_mean = first_sum / seen_count
    spread = second_sum / seen_count - column_mean * column_mean
    standard = ((values - column_mean) * lax.rsqrt(spread + 1e-05) * present).astype(jnp.bfloat16)
    n_samp = lax.axis_size("samp")
    n_var = lax.axis_size("var")
    samples = standard.shape[0] * n_samp
    block_width = standard.shape[1]
    position = lax.axis_index("var")
    raw = {offset: from_behind(standard, "var", -PARTNER_STEP[offset]) for offset in range(1, BAND + 1)}

    arrived, standard_late = lax.optimization_barrier(([raw[d] for d in PROCESS_ORDER], standard))
    owned = {0: reduce_quarters(gram_of(standard_late, standard_late), n_samp)}
    for offset, partner in zip(PROCESS_ORDER, arrived):
        owned[offset] = reduce_quarters(gram_of(standard_late, partner), n_samp)

    row_total = jnp.sum(adjusted_r2(owned[0], samples), 1)
    incoming = jnp.zeros((block_width,), jnp.float32)
    for offset in range(1, BAND + 1):
        step = PARTNER_STEP[offset]
        in_range = ((position + step >= 0) & (position + step < n_var)).astype(jnp.float32)
        adjusted = adjusted_r2(owned[offset], samples) * in_range
        row_total = row_total + jnp.sum(adjusted, 1)
        incoming = incoming + from_behind(jnp.sum(adjusted, 0), "var", step)
    total = row_total + lax.psum_scatter(incoming, "samp", scatter_dimension=0, tiled=True)
    return total / block_width


def solution(mesh):
    placed = (P("samp", "var"), P("samp", "var"))
    return jax.shard_map(
        local, mesh=mesh, in_specs=placed, out_specs=P(("var", "samp")), check_vma=False
    )
```

```python
import jax
import jax.numpy as jnp
from jax import lax
from jax.sharding import PartitionSpec as P

BAND = 3
PARTNER_STEP = {1: 1, 2: 2, 3: -3}
PROCESS_ORDER = (2, 3, 1)


def from_behind(value, axis, steps):
    count = lax.axis_size(axis)
    leading, last = (max(0, -steps), min(count, count - steps))
    return lax.ppermute(value, axis, [(source, source + steps) for source in range(leading, last)])


def adjusted_r2(gram_part, samples):
    correl = gram_part / samples
    squared = correl * correl
    return squared - (1.0 - squared) / (samples - 2)


def gram_of(left, right):
    return lax.dot_general(left, right, (((0,), (0,)), ((), ())), preferred_element_type=jnp.float32)


def reduce_quarters(part, n_samp):
    me = lax.axis_index("samp")
    core, chip = me % 2, me // 2
    quarters = part.reshape(2, 2, part.shape[0] // 4, part.shape[1])
    keep = lax.dynamic_index_in_dim(quarters, core, 1, keepdims=False)
    send = lax.dynamic_index_in_dim(quarters, 1 - core, 1, keepdims=False)
    pairs_core = [(s, s ^ 1) for s in range(n_samp)]
    summed = keep + lax.ppermute(send.astype(jnp.bfloat16), "samp", pairs_core).astype(jnp.float32)
    keep = lax.dynamic_index_in_dim(summed, chip, 0, keepdims=False)
    send = lax.dynamic_index_in_dim(summed, 1 - chip, 0, keepdims=False)
    pairs_chip = [(s, s ^ 2) for s in range(n_samp)]
    return keep + lax.ppermute(send.astype(jnp.bfloat16), "samp", pairs_chip).astype(jnp.float32)


def local(dosages, observed):
    values = dosages.astype(jnp.float32)
    present = observed.astype(jnp.float32)
    seen_count, first_sum, second_sum = lax.psum(
        (jnp.sum(present, 0), jnp.sum(present * values, 0), jnp.sum(present * values * values, 0)),
        "samp",
    )
    seen_count = jnp.maximum(seen_count, 1.0)
    column_mean = first_sum / seen_count
    spread = second_sum / seen_count - column_mean * column_mean
    standard = ((values - column_mean) * lax.rsqrt(spread + 1e-05) * present).astype(jnp.bfloat16)
    n_samp = lax.axis_size("samp")
    n_var = lax.axis_size("var")
    samples = standard.shape[0] * n_samp
    block_width = standard.shape[1]
    position = lax.axis_index("var")
    raw = {offset: from_behind(standard, "var", -PARTNER_STEP[offset]) for offset in range(1, BAND + 1)}

    arrived, gram_same, standard_late = lax.optimization_barrier(
        ([raw[d] for d in PROCESS_ORDER], gram_of(standard, standard), standard)
    )
    owned = {0: reduce_quarters(gram_same, n_samp)}
    for offset, partner in zip(PROCESS_ORDER, arrived):
        owned[offset] = reduce_quarters(gram_of(standard_late, partner), n_samp)

    row_total = jnp.sum(adjusted_r2(owned[0], samples), 1)
    incoming = jnp.zeros((block_width,), jnp.float32)
    for offset in range(1, BAND + 1):
        step = PARTNER_STEP[offset]
        in_range = ((position + step >= 0) & (position + step < n_var)).astype(jnp.float32)
        adjusted = adjusted_r2(owned[offset], samples) * in_range
        row_total = row_total + jnp.sum(adjusted, 1)
        incoming = incoming + from_behind(jnp.sum(adjusted, 0), "var", step)
    total = row_total + lax.psum_scatter(incoming, "samp", scatter_dimension=0, tiled=True)
    return total / block_width


def solution(mesh):
    placed = (P("samp", "var"), P("samp", "var"))
    return jax.shard_map(
        local, mesh=mesh, in_specs=placed, out_specs=P(("var", "samp")), check_vma=False
    )
```

```python
import jax
import jax.numpy as jnp
from jax import lax
from jax.sharding import PartitionSpec as P

BAND = 3
PARTNER_STEP = {1: 1, 2: 2, 3: -3}
PROCESS_ORDER = (2, 3, 1)


def from_behind(value, axis, steps):
    count = lax.axis_size(axis)
    leading, last = (max(0, -steps), min(count, count - steps))
    return lax.ppermute(value, axis, [(source, source + steps) for source in range(leading, last)])


def adjusted_r2(gram_part, samples):
    correl = gram_part / samples
    squared = correl * correl
    return squared - (1.0 - squared) / (samples - 2)


def gram_of(left, right):
    return lax.dot_general(left, right, (((0,), (0,)), ((), ())), preferred_element_type=jnp.float32)


def reduce_quarters(part, n_samp):
    me = lax.axis_index("samp")
    core, chip = me % 2, me // 2
    quarters = part.reshape(2, 2, part.shape[0] // 4, part.shape[1])
    keep = lax.dynamic_index_in_dim(quarters, core, 1, keepdims=False)
    send = lax.dynamic_index_in_dim(quarters, 1 - core, 1, keepdims=False)
    pairs_core = [(s, s ^ 1) for s in range(n_samp)]
    summed = keep + lax.ppermute(send.astype(jnp.bfloat16), "samp", pairs_core).astype(jnp.float32)
    keep = lax.dynamic_index_in_dim(summed, chip, 0, keepdims=False)
    send = lax.dynamic_index_in_dim(summed, 1 - chip, 0, keepdims=False)
    pairs_chip = [(s, s ^ 2) for s in range(n_samp)]
    return keep + lax.ppermute(send.astype(jnp.bfloat16), "samp", pairs_chip).astype(jnp.float32)


def local(dosages, observed):
    values = dosages.astype(jnp.float32)
    present = observed.astype(jnp.float32)
    seen_count, first_sum, second_sum = lax.psum(
        (jnp.sum(present, 0), jnp.sum(present * values, 0), jnp.sum(present * values * values, 0)),
        "samp",
    )
    seen_count = jnp.maximum(seen_count, 1.0)
    column_mean = first_sum / seen_count
    spread = second_sum / seen_count - column_mean * column_mean
    standard = ((values - column_mean) * lax.rsqrt(spread + 1e-05) * present).astype(jnp.bfloat16)
    n_samp = lax.axis_size("samp")
    n_var = lax.axis_size("var")
    samples = standard.shape[0] * n_samp
    block_width = standard.shape[1]
    position = lax.axis_index("var")
    halves = jnp.split(standard, 2, 0)
    raw = {
        offset: [from_behind(half, "var", -PARTNER_STEP[offset]) for half in halves]
        for offset in range(1, BAND + 1)
    }

    arrived, gram_same, standard_late = lax.optimization_barrier(
        ([raw[d] for d in PROCESS_ORDER], gram_of(standard, standard), standard)
    )
    owned = {0: reduce_quarters(gram_same, n_samp)}
    for offset, partner in zip(PROCESS_ORDER, arrived):
        owned[offset] = reduce_quarters(gram_of(standard_late, jnp.concatenate(partner, 0)), n_samp)

    row_total = jnp.sum(adjusted_r2(owned[0], samples), 1)
    incoming = jnp.zeros((block_width,), jnp.float32)
    for offset in range(1, BAND + 1):
        step = PARTNER_STEP[offset]
        in_range = ((position + step >= 0) & (position + step < n_var)).astype(jnp.float32)
        adjusted = adjusted_r2(owned[offset], samples) * in_range
        row_total = row_total + jnp.sum(adjusted, 1)
        incoming = incoming + from_behind(jnp.sum(adjusted, 0), "var", step)
    total = row_total + lax.psum_scatter(incoming, "samp", scatter_dimension=0, tiled=True)
    return total / block_width


def solution(mesh):
    placed = (P("samp", "var"), P("samp", "var"))
    return jax.shard_map(
        local, mesh=mesh, in_specs=placed, out_specs=P(("var", "samp")), check_vma=False
    )
```

```python
import jax
import jax.numpy as jnp
from jax import lax
from jax.sharding import PartitionSpec as P

BAND = 3
PARTNER_STEP = {1: 1, 2: 2, 3: -3}
PROCESS_ORDER = (2, 3, 1)


def from_behind(value, axis, steps):
    count = lax.axis_size(axis)
    leading, last = (max(0, -steps), min(count, count - steps))
    return lax.ppermute(value, axis, [(source, source + steps) for source in range(leading, last)])


def adjusted_r2(gram_part, samples):
    correl = gram_part / samples
    squared = correl * correl
    return squared - (1.0 - squared) / (samples - 2)


def gram_of(left, right):
    return lax.dot_general(left, right, (((0,), (0,)), ((), ())), preferred_element_type=jnp.float32)


def sum_over_core(part, n_samp):
    core = lax.axis_index("samp") % 2
    quarters = part.reshape(2, 2, part.shape[0] // 4, part.shape[1])
    keep = lax.dynamic_index_in_dim(quarters, core, 1, keepdims=False)
    send = lax.dynamic_index_in_dim(quarters, 1 - core, 1, keepdims=False)
    pairs_core = [(s, s ^ 1) for s in range(n_samp)]
    return keep + lax.ppermute(send.astype(jnp.bfloat16), "samp", pairs_core).astype(jnp.float32)


def sum_over_chip(summed, n_samp):
    chip = lax.axis_index("samp") // 2
    keep = lax.dynamic_index_in_dim(summed, chip, 0, keepdims=False)
    send = lax.dynamic_index_in_dim(summed, 1 - chip, 0, keepdims=False)
    pairs_chip = [(s, s ^ 2) for s in range(n_samp)]
    return keep + lax.ppermute(send.astype(jnp.bfloat16), "samp", pairs_chip).astype(jnp.float32)


def local(dosages, observed):
    values = dosages.astype(jnp.float32)
    present = observed.astype(jnp.float32)
    seen_count, first_sum, second_sum = lax.psum(
        (jnp.sum(present, 0), jnp.sum(present * values, 0), jnp.sum(present * values * values, 0)),
        "samp",
    )
    seen_count = jnp.maximum(seen_count, 1.0)
    column_mean = first_sum / seen_count
    spread = second_sum / seen_count - column_mean * column_mean
    standard = ((values - column_mean) * lax.rsqrt(spread + 1e-05) * present).astype(jnp.bfloat16)
    n_samp = lax.axis_size("samp")
    n_var = lax.axis_size("var")
    samples = standard.shape[0] * n_samp
    block_width = standard.shape[1]
    position = lax.axis_index("var")
    halves = jnp.split(standard, 2, 0)
    raw = {
        offset: [from_behind(half, "var", -PARTNER_STEP[offset]) for half in halves]
        for offset in range(1, BAND + 1)
    }

    arrived, gram_same, standard_late = lax.optimization_barrier(
        ([raw[d] for d in PROCESS_ORDER], gram_of(standard, standard), standard)
    )
    core_summed = sum_over_core(gram_same, n_samp)
    arrived, core_summed = lax.optimization_barrier((arrived, core_summed))
    owned = {0: sum_over_chip(core_summed, n_samp)}
    for offset, partner in zip(PROCESS_ORDER, arrived):
        gram = gram_of(standard_late, jnp.concatenate(partner, 0))
        owned[offset] = sum_over_chip(sum_over_core(gram, n_samp), n_samp)

    row_total = jnp.sum(adjusted_r2(owned[0], samples), 1)
    incoming = jnp.zeros((block_width,), jnp.float32)
    for offset in range(1, BAND + 1):
        step = PARTNER_STEP[offset]
        in_range = ((position + step >= 0) & (position + step < n_var)).astype(jnp.float32)
        adjusted = adjusted_r2(owned[offset], samples) * in_range
        row_total = row_total + jnp.sum(adjusted, 1)
        incoming = incoming + from_behind(jnp.sum(adjusted, 0), "var", step)
    total = row_total + lax.psum_scatter(incoming, "samp", scatter_dimension=0, tiled=True)
    return total / block_width


def solution(mesh):
    placed = (P("samp", "var"), P("samp", "var"))
    return jax.shard_map(
        local, mesh=mesh, in_specs=placed, out_specs=P(("var", "samp")), check_vma=False
    )
```

```python
import jax
import jax.numpy as jnp
from jax import lax
from jax.sharding import PartitionSpec as P

BAND = 3
PARTNER_STEP = {1: 1, 2: 2, 3: -3}
PROCESS_ORDER = (2, 3, 1)


def from_behind(value, axis, steps):
    count = lax.axis_size(axis)
    leading, last = (max(0, -steps), min(count, count - steps))
    return lax.ppermute(value, axis, [(source, source + steps) for source in range(leading, last)])


def adjusted_r2(gram_part, samples):
    correl = gram_part / samples
    squared = correl * correl
    return squared - (1.0 - squared) / (samples - 2)


def gram_of(left, right):
    return lax.dot_general(left, right, (((0,), (0,)), ((), ())), preferred_element_type=jnp.float32)


def sum_over_core(part, n_samp):
    core = lax.axis_index("samp") % 2
    rows, cols = part.shape[-2:]
    quarters = part.reshape(part.shape[:-2] + (2, 2, rows // 4, cols))
    keep = lax.dynamic_index_in_dim(quarters, core, quarters.ndim - 3, keepdims=False)
    send = lax.dynamic_index_in_dim(quarters, 1 - core, quarters.ndim - 3, keepdims=False)
    pairs_core = [(s, s ^ 1) for s in range(n_samp)]
    return keep + lax.ppermute(send.astype(jnp.bfloat16), "samp", pairs_core).astype(jnp.float32)


def sum_over_chip(summed, n_samp):
    chip = lax.axis_index("samp") // 2
    keep = lax.dynamic_index_in_dim(summed, chip, summed.ndim - 3, keepdims=False)
    send = lax.dynamic_index_in_dim(summed, 1 - chip, summed.ndim - 3, keepdims=False)
    pairs_chip = [(s, s ^ 2) for s in range(n_samp)]
    return keep + lax.ppermute(send.astype(jnp.bfloat16), "samp", pairs_chip).astype(jnp.float32)


def local(dosages, observed):
    values = dosages.astype(jnp.float32)
    present = observed.astype(jnp.float32)
    seen_count, first_sum, second_sum = lax.psum(
        (jnp.sum(present, 0), jnp.sum(present * values, 0), jnp.sum(present * values * values, 0)),
        "samp",
    )
    seen_count = jnp.maximum(seen_count, 1.0)
    column_mean = first_sum / seen_count
    spread = second_sum / seen_count - column_mean * column_mean
    standard = ((values - column_mean) * lax.rsqrt(spread + 1e-05) * present).astype(jnp.bfloat16)
    n_samp = lax.axis_size("samp")
    n_var = lax.axis_size("var")
    samples = standard.shape[0] * n_samp
    block_width = standard.shape[1]
    position = lax.axis_index("var")
    halves = jnp.split(standard, 2, 0)
    raw = {
        offset: [from_behind(half, "var", -PARTNER_STEP[offset]) for half in halves]
        for offset in range(1, BAND + 1)
    }

    arrived, gram_same, standard_late = lax.optimization_barrier(
        ([raw[d] for d in PROCESS_ORDER], gram_of(standard, standard), standard)
    )
    core_summed = sum_over_core(gram_same, n_samp)
    arrived, core_summed = lax.optimization_barrier((arrived, core_summed))
    owned = {0: sum_over_chip(core_summed, n_samp)}
    grams = jnp.stack([gram_of(standard_late, jnp.concatenate(partner, 0)) for partner in arrived])
    reduced = sum_over_chip(sum_over_core(grams, n_samp), n_samp)
    for index, offset in enumerate(PROCESS_ORDER):
        owned[offset] = reduced[index]

    row_total = jnp.sum(adjusted_r2(owned[0], samples), 1)
    incoming = jnp.zeros((block_width,), jnp.float32)
    for offset in range(1, BAND + 1):
        step = PARTNER_STEP[offset]
        in_range = ((position + step >= 0) & (position + step < n_var)).astype(jnp.float32)
        adjusted = adjusted_r2(owned[offset], samples) * in_range
        row_total = row_total + jnp.sum(adjusted, 1)
        incoming = incoming + from_behind(jnp.sum(adjusted, 0), "var", step)
    total = row_total + lax.psum_scatter(incoming, "samp", scatter_dimension=0, tiled=True)
    return total / block_width


def solution(mesh):
    placed = (P("samp", "var"), P("samp", "var"))
    return jax.shard_map(
        local, mesh=mesh, in_specs=placed, out_specs=P(("var", "samp")), check_vma=False
    )
```

```python
import jax
import jax.numpy as jnp
from jax import lax
from jax.sharding import PartitionSpec as P

BAND = 3
PARTNER_STEP = {1: 1, 2: 2, 3: -3}
PROCESS_ORDER = (2, 3, 1)


def from_behind(value, axis, steps):
    count = lax.axis_size(axis)
    leading, last = (max(0, -steps), min(count, count - steps))
    return lax.ppermute(value, axis, [(source, source + steps) for source in range(leading, last)])


def adjusted_r2(gram_part, samples):
    correl = gram_part / samples
    squared = correl * correl
    return squared - (1.0 - squared) / (samples - 2)


def gram_of(left, right):
    return lax.dot_general(left, right, (((0,), (0,)), ((), ())), preferred_element_type=jnp.float32)


def reduce_quarters(part, n_samp):
    me = lax.axis_index("samp")
    core, chip = me % 2, me // 2
    quarters = part.reshape(2, 2, part.shape[0] // 4, part.shape[1])
    keep = lax.dynamic_index_in_dim(quarters, core, 1, keepdims=False)
    send = lax.dynamic_index_in_dim(quarters, 1 - core, 1, keepdims=False)
    pairs_core = [(s, s ^ 1) for s in range(n_samp)]
    summed = keep + lax.ppermute(send.astype(jnp.bfloat16), "samp", pairs_core).astype(jnp.float32)
    keep = lax.dynamic_index_in_dim(summed, chip, 0, keepdims=False)
    send = lax.dynamic_index_in_dim(summed, 1 - chip, 0, keepdims=False)
    pairs_chip = [(s, s ^ 2) for s in range(n_samp)]
    return keep + lax.ppermute(send.astype(jnp.bfloat16), "samp", pairs_chip).astype(jnp.float32)


def reduce_to_owner(part, owner, n_samp):
    pairs_core = [(s, s ^ 1) for s in range(n_samp) if (s & 1) != (owner & 1)]
    summed = part + lax.ppermute(part.astype(jnp.bfloat16), "samp", pairs_core).astype(jnp.float32)
    pairs_chip = [(owner ^ 2, owner)]
    return summed + lax.ppermute(summed.astype(jnp.bfloat16), "samp", pairs_chip).astype(jnp.float32)


def local(dosages, observed):
    values = dosages.astype(jnp.float32)
    present = observed.astype(jnp.float32)
    seen_count, first_sum, second_sum = lax.psum(
        (jnp.sum(present, 0), jnp.sum(present * values, 0), jnp.sum(present * values * values, 0)),
        "samp",
    )
    seen_count = jnp.maximum(seen_count, 1.0)
    column_mean = first_sum / seen_count
    spread = second_sum / seen_count - column_mean * column_mean
    standard = ((values - column_mean) * lax.rsqrt(spread + 1e-05) * present).astype(jnp.bfloat16)
    n_samp = lax.axis_size("samp")
    n_var = lax.axis_size("var")
    samples = standard.shape[0] * n_samp
    block_width = standard.shape[1]
    position = lax.axis_index("var")
    raw = {offset: from_behind(standard, "var", -PARTNER_STEP[offset]) for offset in range(1, BAND + 1)}

    same_total = reduce_to_owner(gram_of(standard, standard), 0, n_samp)
    arrived, same_total, standard_late = lax.optimization_barrier(
        ([raw[d] for d in PROCESS_ORDER], same_total, standard)
    )
    owned = {}
    for offset, partner in zip(PROCESS_ORDER, arrived):
        owned[offset] = reduce_quarters(gram_of(standard_late, partner), n_samp)

    me = lax.axis_index("samp")
    incoming = jnp.sum(adjusted_r2(same_total, samples), 1) * (me == 0).astype(jnp.float32)
    row_total = jnp.zeros((block_width // n_samp,), jnp.float32)
    for offset in range(1, BAND + 1):
        step = PARTNER_STEP[offset]
        in_range = ((position + step >= 0) & (position + step < n_var)).astype(jnp.float32)
        adjusted = adjusted_r2(owned[offset], samples) * in_range
        row_total = row_total + jnp.sum(adjusted, 1)
        incoming = incoming + from_behind(jnp.sum(adjusted, 0), "var", step)
    total = row_total + lax.psum_scatter(incoming, "samp", scatter_dimension=0, tiled=True)
    return total / block_width


def solution(mesh):
    placed = (P("samp", "var"), P("samp", "var"))
    return jax.shard_map(
        local, mesh=mesh, in_specs=placed, out_specs=P(("var", "samp")), check_vma=False
    )
```

```python
import jax
import jax.numpy as jnp
from jax import lax
from jax.sharding import PartitionSpec as P

BAND = 3
PARTNER_STEP = {1: 1, 2: 2, 3: -3}
LATE_OFFSETS = (2, 3)


def from_behind(value, axis, steps):
    count = lax.axis_size(axis)
    leading, last = (max(0, -steps), min(count, count - steps))
    return lax.ppermute(value, axis, [(source, source + steps) for source in range(leading, last)])


def adjusted_r2(gram_part, samples):
    correl = gram_part / samples
    squared = correl * correl
    return squared - (1.0 - squared) / (samples - 2)


def gram_of(left, right):
    return lax.dot_general(left, right, (((0,), (0,)), ((), ())), preferred_element_type=jnp.float32)


def reduce_quarters(part, n_samp):
    me = lax.axis_index("samp")
    core, chip = me % 2, me // 2
    quarters = part.reshape(2, 2, part.shape[0] // 4, part.shape[1])
    keep = lax.dynamic_index_in_dim(quarters, core, 1, keepdims=False)
    send = lax.dynamic_index_in_dim(quarters, 1 - core, 1, keepdims=False)
    pairs_core = [(s, s ^ 1) for s in range(n_samp)]
    summed = keep + lax.ppermute(send.astype(jnp.bfloat16), "samp", pairs_core).astype(jnp.float32)
    keep = lax.dynamic_index_in_dim(summed, chip, 0, keepdims=False)
    send = lax.dynamic_index_in_dim(summed, 1 - chip, 0, keepdims=False)
    pairs_chip = [(s, s ^ 2) for s in range(n_samp)]
    return keep + lax.ppermute(send.astype(jnp.bfloat16), "samp", pairs_chip).astype(jnp.float32)


def reduce_to_owner(part, owner, n_samp):
    pairs_core = [(s, s ^ 1) for s in range(n_samp) if (s & 1) != (owner & 1)]
    summed = part + lax.ppermute(part.astype(jnp.bfloat16), "samp", pairs_core).astype(jnp.float32)
    pairs_chip = [(owner ^ 2, owner)]
    return summed + lax.ppermute(summed.astype(jnp.bfloat16), "samp", pairs_chip).astype(jnp.float32)


def local(dosages, observed):
    values = dosages.astype(jnp.float32)
    present = observed.astype(jnp.float32)
    seen_count, first_sum, second_sum = lax.psum(
        (jnp.sum(present, 0), jnp.sum(present * values, 0), jnp.sum(present * values * values, 0)),
        "samp",
    )
    seen_count = jnp.maximum(seen_count, 1.0)
    column_mean = first_sum / seen_count
    spread = second_sum / seen_count - column_mean * column_mean
    standard = ((values - column_mean) * lax.rsqrt(spread + 1e-05) * present).astype(jnp.bfloat16)
    n_samp = lax.axis_size("samp")
    n_var = lax.axis_size("var")
    samples = standard.shape[0] * n_samp
    block_width = standard.shape[1]
    position = lax.axis_index("var")
    raw = {offset: from_behind(standard, "var", -PARTNER_STEP[offset]) for offset in range(1, BAND + 1)}

    same_total = reduce_to_owner(gram_of(standard, standard), 0, n_samp)
    next_total = reduce_to_owner(gram_of(standard, raw[1]), 1, n_samp)
    arrived, same_total, next_total, standard_late = lax.optimization_barrier(
        ([raw[d] for d in LATE_OFFSETS], same_total, next_total, standard)
    )
    owned = {}
    for offset, partner in zip(LATE_OFFSETS, arrived):
        owned[offset] = reduce_quarters(gram_of(standard_late, partner), n_samp)

    me = lax.axis_index("samp")
    incoming = jnp.sum(adjusted_r2(same_total, samples), 1) * (me == 0).astype(jnp.float32)
    next_in_range = (position + PARTNER_STEP[1] < n_var).astype(jnp.float32)
    next_adjusted = adjusted_r2(next_total, samples) * (next_in_range * (me == 1).astype(jnp.float32))
    incoming = incoming + jnp.sum(next_adjusted, 1)
    incoming = incoming + from_behind(jnp.sum(next_adjusted, 0), "var", PARTNER_STEP[1])
    row_total = jnp.zeros((block_width // n_samp,), jnp.float32)
    for offset in LATE_OFFSETS:
        step = PARTNER_STEP[offset]
        in_range = ((position + step >= 0) & (position + step < n_var)).astype(jnp.float32)
        adjusted = adjusted_r2(owned[offset], samples) * in_range
        row_total = row_total + jnp.sum(adjusted, 1)
        incoming = incoming + from_behind(jnp.sum(adjusted, 0), "var", step)
    total = row_total + lax.psum_scatter(incoming, "samp", scatter_dimension=0, tiled=True)
    return total / block_width


def solution(mesh):
    placed = (P("samp", "var"), P("samp", "var"))
    return jax.shard_map(
        local, mesh=mesh, in_specs=placed, out_specs=P(("var", "samp")), check_vma=False
    )
```

```python
import jax
import jax.numpy as jnp
from jax import lax
from jax.sharding import PartitionSpec as P

BAND = 3
PARTNER_STEP = {1: 1, 2: 2, 3: -3}
LATE_OFFSETS = (2, 3)


def from_behind(value, axis, steps):
    count = lax.axis_size(axis)
    leading, last = (max(0, -steps), min(count, count - steps))
    return lax.ppermute(value, axis, [(source, source + steps) for source in range(leading, last)])


def adjusted_r2(gram_part, samples):
    correl = gram_part / samples
    squared = correl * correl
    return squared - (1.0 - squared) / (samples - 2)


def gram_of(left, right):
    return lax.dot_general(left, right, (((0,), (0,)), ((), ())), preferred_element_type=jnp.float32)


def reduce_quarters(part, n_samp):
    me = lax.axis_index("samp")
    core, chip = me % 2, me // 2
    quarters = part.reshape(2, 2, part.shape[0] // 4, part.shape[1])
    keep = lax.dynamic_index_in_dim(quarters, core, 1, keepdims=False)
    send = lax.dynamic_index_in_dim(quarters, 1 - core, 1, keepdims=False)
    pairs_core = [(s, s ^ 1) for s in range(n_samp)]
    summed = keep + lax.ppermute(send.astype(jnp.bfloat16), "samp", pairs_core).astype(jnp.float32)
    keep = lax.dynamic_index_in_dim(summed, chip, 0, keepdims=False)
    send = lax.dynamic_index_in_dim(summed, 1 - chip, 0, keepdims=False)
    pairs_chip = [(s, s ^ 2) for s in range(n_samp)]
    return keep + lax.ppermute(send.astype(jnp.bfloat16), "samp", pairs_chip).astype(jnp.float32)


def reduce_to_owner(part, owner, n_samp):
    pairs_core = [(s, s ^ 1) for s in range(n_samp) if (s & 1) != (owner & 1)]
    summed = part + lax.ppermute(part.astype(jnp.bfloat16), "samp", pairs_core).astype(jnp.float32)
    pairs_chip = [(owner ^ 2, owner)]
    return summed + lax.ppermute(summed.astype(jnp.bfloat16), "samp", pairs_chip).astype(jnp.float32)


def local(dosages, observed):
    values = dosages.astype(jnp.float32)
    present = observed.astype(jnp.float32)
    seen_count, first_sum, second_sum = lax.psum(
        (jnp.sum(present, 0), jnp.sum(present * values, 0), jnp.sum(present * values * values, 0)),
        "samp",
    )
    seen_count = jnp.maximum(seen_count, 1.0)
    column_mean = first_sum / seen_count
    spread = second_sum / seen_count - column_mean * column_mean
    standard = ((values - column_mean) * lax.rsqrt(spread + 1e-05) * present).astype(jnp.bfloat16)
    n_samp = lax.axis_size("samp")
    n_var = lax.axis_size("var")
    samples = standard.shape[0] * n_samp
    block_width = standard.shape[1]
    position = lax.axis_index("var")
    raw = {offset: from_behind(standard, "var", -PARTNER_STEP[offset]) for offset in range(1, BAND + 1)}

    same_total = reduce_to_owner(gram_of(standard, standard), 0, n_samp)
    next_gram = gram_of(standard, raw[1])
    arrived, same_total, next_gram, standard_late = lax.optimization_barrier(
        ([raw[d] for d in LATE_OFFSETS], same_total, next_gram, standard)
    )
    owned = {1: reduce_quarters(next_gram, n_samp)}
    for offset, partner in zip(LATE_OFFSETS, arrived):
        owned[offset] = reduce_quarters(gram_of(standard_late, partner), n_samp)

    me = lax.axis_index("samp")
    incoming = jnp.sum(adjusted_r2(same_total, samples), 1) * (me == 0).astype(jnp.float32)
    row_total = jnp.zeros((block_width // n_samp,), jnp.float32)
    for offset in range(1, BAND + 1):
        step = PARTNER_STEP[offset]
        in_range = ((position + step >= 0) & (position + step < n_var)).astype(jnp.float32)
        adjusted = adjusted_r2(owned[offset], samples) * in_range
        row_total = row_total + jnp.sum(adjusted, 1)
        incoming = incoming + from_behind(jnp.sum(adjusted, 0), "var", step)
    total = row_total + lax.psum_scatter(incoming, "samp", scatter_dimension=0, tiled=True)
    return total / block_width


def solution(mesh):
    placed = (P("samp", "var"), P("samp", "var"))
    return jax.shard_map(
        local, mesh=mesh, in_specs=placed, out_specs=P(("var", "samp")), check_vma=False
    )
```

```python
import jax
import jax.numpy as jnp
from jax import lax
from jax.sharding import PartitionSpec as P

BAND = 3
PARTNER_STEP = {1: 1, 2: 2, 3: 3}
PROCESS_ORDER = (2, 3, 1)


def from_behind(value, axis, steps):
    count = lax.axis_size(axis)
    leading, last = (max(0, -steps), min(count, count - steps))
    return lax.ppermute(value, axis, [(source, source + steps) for source in range(leading, last)])


def adjusted_r2(gram_part, samples):
    correl = gram_part / samples
    squared = correl * correl
    return squared - (1.0 - squared) / (samples - 2)


def gram_of(left, right):
    return lax.dot_general(left, right, (((0,), (0,)), ((), ())), preferred_element_type=jnp.float32)


def reduce_quarters(part, n_samp):
    me = lax.axis_index("samp")
    core, chip = me % 2, me // 2
    quarters = part.reshape(2, 2, part.shape[0] // 4, part.shape[1])
    keep = lax.dynamic_index_in_dim(quarters, core, 1, keepdims=False)
    send = lax.dynamic_index_in_dim(quarters, 1 - core, 1, keepdims=False)
    pairs_core = [(s, s ^ 1) for s in range(n_samp)]
    summed = keep + lax.ppermute(send.astype(jnp.bfloat16), "samp", pairs_core).astype(jnp.float32)
    keep = lax.dynamic_index_in_dim(summed, chip, 0, keepdims=False)
    send = lax.dynamic_index_in_dim(summed, 1 - chip, 0, keepdims=False)
    pairs_chip = [(s, s ^ 2) for s in range(n_samp)]
    return keep + lax.ppermute(send.astype(jnp.bfloat16), "samp", pairs_chip).astype(jnp.float32)


def reduce_to_owner(part, owner, n_samp):
    pairs_core = [(s, s ^ 1) for s in range(n_samp) if (s & 1) != (owner & 1)]
    summed = part + lax.ppermute(part.astype(jnp.bfloat16), "samp", pairs_core).astype(jnp.float32)
    pairs_chip = [(owner ^ 2, owner)]
    return summed + lax.ppermute(summed.astype(jnp.bfloat16), "samp", pairs_chip).astype(jnp.float32)


def local(dosages, observed):
    values = dosages.astype(jnp.float32)
    present = observed.astype(jnp.float32)
    seen_count, first_sum, second_sum = lax.psum(
        (jnp.sum(present, 0), jnp.sum(present * values, 0), jnp.sum(present * values * values, 0)),
        "samp",
    )
    seen_count = jnp.maximum(seen_count, 1.0)
    column_mean = first_sum / seen_count
    spread = second_sum / seen_count - column_mean * column_mean
    standard = ((values - column_mean) * lax.rsqrt(spread + 1e-05) * present).astype(jnp.bfloat16)
    n_samp = lax.axis_size("samp")
    n_var = lax.axis_size("var")
    samples = standard.shape[0] * n_samp
    block_width = standard.shape[1]
    position = lax.axis_index("var")
    raw = {offset: from_behind(standard, "var", -PARTNER_STEP[offset]) for offset in range(1, BAND + 1)}

    same_total = reduce_to_owner(gram_of(standard, standard), 0, n_samp)
    arrived, same_total, standard_late = lax.optimization_barrier(
        ([raw[d] for d in PROCESS_ORDER], same_total, standard)
    )
    owned = {}
    for offset, partner in zip(PROCESS_ORDER, arrived):
        owned[offset] = reduce_quarters(gram_of(standard_late, partner), n_samp)

    me = lax.axis_index("samp")
    incoming = jnp.sum(adjusted_r2(same_total, samples), 1) * (me == 0).astype(jnp.float32)
    row_total = jnp.zeros((block_width // n_samp,), jnp.float32)
    for offset in range(1, BAND + 1):
        step = PARTNER_STEP[offset]
        in_range = ((position + step >= 0) & (position + step < n_var)).astype(jnp.float32)
        adjusted = adjusted_r2(owned[offset], samples) * in_range
        row_total = row_total + jnp.sum(adjusted, 1)
        incoming = incoming + from_behind(jnp.sum(adjusted, 0), "var", step)
    total = row_total + lax.psum_scatter(incoming, "samp", scatter_dimension=0, tiled=True)
    return total / block_width


def solution(mesh):
    placed = (P("samp", "var"), P("samp", "var"))
    return jax.shard_map(
        local, mesh=mesh, in_specs=placed, out_specs=P(("var", "samp")), check_vma=False
    )
```

```python
import jax
import jax.numpy as jnp
from jax import lax
from jax.sharding import PartitionSpec as P

BAND = 3
PARTNER_STEP = {1: 1, 2: 2, 3: -3}
PROCESS_ORDER = (2, 3, 1)


def from_behind(value, axis, steps):
    count = lax.axis_size(axis)
    leading, last = (max(0, -steps), min(count, count - steps))
    return lax.ppermute(value, axis, [(source, source + steps) for source in range(leading, last)])


def adjusted_r2(gram_part, samples):
    correl = gram_part / samples
    squared = correl * correl
    return squared - (1.0 - squared) / (samples - 2)


def gram_of(left, right):
    return lax.dot_general(left, right, (((0,), (0,)), ((), ())), preferred_element_type=jnp.float32)


def reduce_quarters(part, n_samp):
    me = lax.axis_index("samp")
    core, chip = me % 2, me // 2
    quarters = part.reshape(2, 2, part.shape[0] // 4, part.shape[1])
    keep = lax.dynamic_index_in_dim(quarters, core, 1, keepdims=False)
    send = lax.dynamic_index_in_dim(quarters, 1 - core, 1, keepdims=False)
    pairs_core = [(s, s ^ 1) for s in range(n_samp)]
    summed = keep + lax.ppermute(send.astype(jnp.bfloat16), "samp", pairs_core).astype(jnp.float32)
    keep = lax.dynamic_index_in_dim(summed, chip, 0, keepdims=False)
    send = lax.dynamic_index_in_dim(summed, 1 - chip, 0, keepdims=False)
    pairs_chip = [(s, s ^ 2) for s in range(n_samp)]
    return keep + lax.ppermute(send.astype(jnp.bfloat16), "samp", pairs_chip).astype(jnp.float32)


def reduce_to_owner(part, owner, n_samp):
    pairs_core = [(s, s ^ 1) for s in range(n_samp) if (s & 1) != (owner & 1)]
    summed = part + lax.ppermute(part.astype(jnp.bfloat16), "samp", pairs_core).astype(jnp.float32)
    pairs_chip = [(owner ^ 2, owner)]
    return summed + lax.ppermute(summed.astype(jnp.bfloat16), "samp", pairs_chip).astype(jnp.float32)


def local(dosages, observed):
    values = dosages.astype(jnp.float32)
    present = observed.astype(jnp.float32)
    n_samp = lax.axis_size("samp")
    n_var = lax.axis_size("var")
    position = lax.axis_index("var")
    partial = jnp.stack([jnp.sum(present, 0), jnp.sum(present * values, 0), jnp.sum(present * values * values, 0)])
    partner_partials = [from_behind(partial, "var", -PARTNER_STEP[d]) for d in PROCESS_ORDER]
    coded = jnp.where(observed != 0, dosages, jnp.asarray(-1, dosages.dtype))
    coded, partner_partials = lax.optimization_barrier((coded, partner_partials))
    raw = {offset: from_behind(coded, "var", -PARTNER_STEP[offset]) for offset in range(1, BAND + 1)}
    stats = lax.psum(jnp.stack([partial] + partner_partials), "samp")
    seen_count = jnp.maximum(stats[:, 0], 1.0)
    column_mean = stats[:, 1] / seen_count
    spread = stats[:, 2] / seen_count - column_mean * column_mean
    scale = lax.rsqrt(spread + 1e-05)
    standard = ((values - column_mean[0]) * scale[0] * present).astype(jnp.bfloat16)
    samples = standard.shape[0] * n_samp
    block_width = standard.shape[1]

    same_total = reduce_to_owner(gram_of(standard, standard), 0, n_samp)
    arrived, same_total, standard_late = lax.optimization_barrier(
        ([raw[d] for d in PROCESS_ORDER], same_total, standard)
    )
    owned = {}
    for index, (offset, coded_partner) in enumerate(zip(PROCESS_ORDER, arrived)):
        partner_values = coded_partner.astype(jnp.float32)
        partner_present = (partner_values >= 0).astype(jnp.float32)
        partner = (
            (partner_values - column_mean[index + 1]) * scale[index + 1] * partner_present
        ).astype(jnp.bfloat16)
        owned[offset] = reduce_quarters(gram_of(standard_late, partner), n_samp)

    me = lax.axis_index("samp")
    incoming = jnp.sum(adjusted_r2(same_total, samples), 1) * (me == 0).astype(jnp.float32)
    row_total = jnp.zeros((block_width // n_samp,), jnp.float32)
    for offset in range(1, BAND + 1):
        step = PARTNER_STEP[offset]
        in_range = ((position + step >= 0) & (position + step < n_var)).astype(jnp.float32)
        adjusted = adjusted_r2(owned[offset], samples) * in_range
        row_total = row_total + jnp.sum(adjusted, 1)
        incoming = incoming + from_behind(jnp.sum(adjusted, 0), "var", step)
    total = row_total + lax.psum_scatter(incoming, "samp", scatter_dimension=0, tiled=True)
    return total / block_width


def solution(mesh):
    placed = (P("samp", "var"), P("samp", "var"))
    return jax.shard_map(
        local, mesh=mesh, in_specs=placed, out_specs=P(("var", "samp")), check_vma=False
    )
```

```python
import jax
import jax.numpy as jnp
from jax import lax
from jax.sharding import PartitionSpec as P

BAND = 3
PARTNER_STEP = {1: 1, 2: 2, 3: -3}
PROCESS_ORDER = (2, 3, 1)


def from_behind(value, axis, steps):
    count = lax.axis_size(axis)
    leading, last = (max(0, -steps), min(count, count - steps))
    return lax.ppermute(value, axis, [(source, source + steps) for source in range(leading, last)])


def adjusted_r2(gram_part, samples):
    correl = gram_part / samples
    squared = correl * correl
    return squared - (1.0 - squared) / (samples - 2)


def gram_of(left, right):
    return lax.dot_general(left, right, (((0,), (0,)), ((), ())), preferred_element_type=jnp.float32)


def reduce_quarters(part, n_samp):
    me = lax.axis_index("samp")
    core, chip = me % 2, me // 2
    quarters = part.reshape(2, 2, part.shape[0] // 4, part.shape[1])
    keep = lax.dynamic_index_in_dim(quarters, core, 1, keepdims=False)
    send = lax.dynamic_index_in_dim(quarters, 1 - core, 1, keepdims=False)
    pairs_core = [(s, s ^ 1) for s in range(n_samp)]
    summed = keep + lax.ppermute(send.astype(jnp.bfloat16), "samp", pairs_core).astype(jnp.float32)
    keep = lax.dynamic_index_in_dim(summed, chip, 0, keepdims=False)
    send = lax.dynamic_index_in_dim(summed, 1 - chip, 0, keepdims=False)
    pairs_chip = [(s, s ^ 2) for s in range(n_samp)]
    return keep + lax.ppermute(send.astype(jnp.bfloat16), "samp", pairs_chip).astype(jnp.float32)


def reduce_to_owner(part, owner, n_samp):
    pairs_core = [(s, s ^ 1) for s in range(n_samp) if (s & 1) != (owner & 1)]
    summed = part + lax.ppermute(part.astype(jnp.bfloat16), "samp", pairs_core).astype(jnp.float32)
    pairs_chip = [(owner ^ 2, owner)]
    return summed + lax.ppermute(summed.astype(jnp.bfloat16), "samp", pairs_chip).astype(jnp.float32)


def local(dosages, observed):
    values = dosages.astype(jnp.float32)
    present = observed.astype(jnp.float32)
    n_samp = lax.axis_size("samp")
    n_var = lax.axis_size("var")
    position = lax.axis_index("var")
    partial = jnp.stack([jnp.sum(present, 0), jnp.sum(present * values, 0), jnp.sum(present * values * values, 0)])
    partner_partials = [from_behind(partial, "var", -PARTNER_STEP[d]) for d in PROCESS_ORDER]
    coded = jnp.where(observed != 0, dosages, jnp.asarray(-1, dosages.dtype))
    coded, partner_partials = lax.optimization_barrier((coded, partner_partials))
    raw = {offset: from_behind(coded, "var", -PARTNER_STEP[offset]) for offset in range(1, BAND + 1)}
    stats = lax.psum(jnp.stack([partial] + partner_partials), "samp")
    seen_count = jnp.maximum(stats[:, 0], 1.0)
    column_mean = stats[:, 1] / seen_count
    spread = stats[:, 2] / seen_count - column_mean * column_mean
    scale = lax.rsqrt(spread + 1e-05)
    standard = ((values - column_mean[0]) * scale[0] * present).astype(jnp.bfloat16)
    samples = standard.shape[0] * n_samp
    block_width = standard.shape[1]

    same_total = reduce_to_owner(gram_of(standard, standard), 0, n_samp)
    arrived, same_total, standard_late = lax.optimization_barrier(
        ([raw[d] for d in PROCESS_ORDER], same_total, standard)
    )
    owned = {}
    for index, (offset, coded_partner) in enumerate(zip(PROCESS_ORDER, arrived)):
        partner_values = coded_partner.astype(jnp.float32)
        partner_present = (partner_values >= 0).astype(jnp.float32)
        partner = (
            (partner_values - column_mean[index + 1]) * scale[index + 1] * partner_present
        ).astype(jnp.bfloat16)
        owned[offset] = reduce_quarters(gram_of(standard_late, partner), n_samp)

    me = lax.axis_index("samp")
    incoming = jnp.sum(adjusted_r2(same_total, samples), 1) * (me == 0).astype(jnp.float32)
    row_total = jnp.zeros((block_width // n_samp,), jnp.float32)
    for offset in range(1, BAND + 1):
        step = PARTNER_STEP[offset]
        in_range = ((position + step >= 0) & (position + step < n_var)).astype(jnp.float32)
        adjusted = adjusted_r2(owned[offset], samples) * in_range
        row_total = row_total + jnp.sum(adjusted, 1)
        incoming = incoming + from_behind(jnp.sum(adjusted, 0), "var", step)
    core, chip = me % 2, me // 2
    halves = incoming.reshape(2, 2, block_width // n_samp)
    keep = lax.dynamic_index_in_dim(halves, core, 1, keepdims=False)
    send = lax.dynamic_index_in_dim(halves, 1 - core, 1, keepdims=False)
    summed = keep + lax.ppermute(send, "samp", [(s, s ^ 1) for s in range(n_samp)])
    keep = lax.dynamic_index_in_dim(summed, chip, 0, keepdims=False)
    send = lax.dynamic_index_in_dim(summed, 1 - chip, 0, keepdims=False)
    total = row_total + keep + lax.ppermute(send, "samp", [(s, s ^ 2) for s in range(n_samp)])
    return total / block_width


def solution(mesh):
    placed = (P("samp", "var"), P("samp", "var"))
    return jax.shard_map(
        local, mesh=mesh, in_specs=placed, out_specs=P(("var", "samp")), check_vma=False
    )
```

```python
import jax
import jax.numpy as jnp
from jax import lax
from jax.sharding import PartitionSpec as P

BAND = 3
PARTNER_STEP = {1: 1, 2: 2, 3: -3}
PROCESS_ORDER = (2, 3, 1)


def from_behind(value, axis, steps):
    count = lax.axis_size(axis)
    leading, last = (max(0, -steps), min(count, count - steps))
    return lax.ppermute(value, axis, [(source, source + steps) for source in range(leading, last)])


def adjusted_r2(gram_part, samples):
    correl = gram_part / samples
    squared = correl * correl
    return squared - (1.0 - squared) / (samples - 2)


def gram_of(left, right):
    return lax.dot_general(left, right, (((0,), (0,)), ((), ())), preferred_element_type=jnp.float32)


def reduce_quarters(part, n_samp):
    me = lax.axis_index("samp")
    core, chip = me % 2, me // 2
    quarters = part.reshape(2, 2, part.shape[0] // 4, part.shape[1])
    keep = lax.dynamic_index_in_dim(quarters, core, 1, keepdims=False)
    send = lax.dynamic_index_in_dim(quarters, 1 - core, 1, keepdims=False)
    pairs_core = [(s, s ^ 1) for s in range(n_samp)]
    summed = keep + lax.ppermute(send.astype(jnp.bfloat16), "samp", pairs_core).astype(jnp.float32)
    keep = lax.dynamic_index_in_dim(summed, chip, 0, keepdims=False)
    send = lax.dynamic_index_in_dim(summed, 1 - chip, 0, keepdims=False)
    pairs_chip = [(s, s ^ 2) for s in range(n_samp)]
    return keep + lax.ppermute(send.astype(jnp.bfloat16), "samp", pairs_chip).astype(jnp.float32)


def reduce_to_owner(part, owner, n_samp):
    pairs_core = [(s, s ^ 1) for s in range(n_samp) if (s & 1) != (owner & 1)]
    summed = part + lax.ppermute(part.astype(jnp.bfloat16), "samp", pairs_core).astype(jnp.float32)
    pairs_chip = [(owner ^ 2, owner)]
    return summed + lax.ppermute(summed.astype(jnp.bfloat16), "samp", pairs_chip).astype(jnp.float32)


def local(dosages, observed):
    values = dosages.astype(jnp.float32)
    present = observed.astype(jnp.float32)
    n_samp = lax.axis_size("samp")
    n_var = lax.axis_size("var")
    position = lax.axis_index("var")
    partial = jnp.stack([jnp.sum(present, 0), jnp.sum(present * values, 0), jnp.sum(present * values * values, 0)])
    partner_partials = [from_behind(partial, "var", -PARTNER_STEP[d]) for d in PROCESS_ORDER]
    coded = jnp.where(observed != 0, dosages, jnp.asarray(-1, dosages.dtype))
    coded, partner_partials = lax.optimization_barrier((coded, partner_partials))
    raw = {offset: from_behind(coded, "var", -PARTNER_STEP[offset]) for offset in range(1, BAND + 1)}
    stats = lax.psum(jnp.stack([partial] + partner_partials), "samp")
    seen_count = jnp.maximum(stats[:, 0], 1.0)
    column_mean = stats[:, 1] / seen_count
    spread = stats[:, 2] / seen_count - column_mean * column_mean
    scale = lax.rsqrt(spread + 1e-05)
    standard = ((values - column_mean[0]) * scale[0] * present).astype(jnp.bfloat16)
    samples = standard.shape[0] * n_samp
    block_width = standard.shape[1]

    same_total = reduce_to_owner(gram_of(standard, standard), 0, n_samp)
    arrived, same_total, standard_late = lax.optimization_barrier(
        ([raw[d] for d in PROCESS_ORDER], same_total, standard)
    )
    owned = {}
    for index, offset in enumerate(PROCESS_ORDER):
        coded_partner = arrived[index]
        partner_values = coded_partner.astype(jnp.float32)
        partner_present = (partner_values >= 0).astype(jnp.float32)
        partner = (
            (partner_values - column_mean[index + 1]) * scale[index + 1] * partner_present
        ).astype(jnp.bfloat16)
        owned[offset] = reduce_quarters(gram_of(standard_late, partner), n_samp)
        if index == 0:
            rest, owned[offset] = lax.optimization_barrier((arrived[1:], owned[offset]))
            arrived = arrived[:1] + list(rest)

    me = lax.axis_index("samp")
    incoming = jnp.sum(adjusted_r2(same_total, samples), 1) * (me == 0).astype(jnp.float32)
    row_total = jnp.zeros((block_width // n_samp,), jnp.float32)
    for offset in range(1, BAND + 1):
        step = PARTNER_STEP[offset]
        in_range = ((position + step >= 0) & (position + step < n_var)).astype(jnp.float32)
        adjusted = adjusted_r2(owned[offset], samples) * in_range
        row_total = row_total + jnp.sum(adjusted, 1)
        incoming = incoming + from_behind(jnp.sum(adjusted, 0), "var", step)
    core, chip = me % 2, me // 2
    halves = incoming.reshape(2, 2, block_width // n_samp)
    keep = lax.dynamic_index_in_dim(halves, core, 1, keepdims=False)
    send = lax.dynamic_index_in_dim(halves, 1 - core, 1, keepdims=False)
    summed = keep + lax.ppermute(send, "samp", [(s, s ^ 1) for s in range(n_samp)])
    keep = lax.dynamic_index_in_dim(summed, chip, 0, keepdims=False)
    send = lax.dynamic_index_in_dim(summed, 1 - chip, 0, keepdims=False)
    total = row_total + keep + lax.ppermute(send, "samp", [(s, s ^ 2) for s in range(n_samp)])
    return total / block_width


def solution(mesh):
    placed = (P("samp", "var"), P("samp", "var"))
    return jax.shard_map(
        local, mesh=mesh, in_specs=placed, out_specs=P(("var", "samp")), check_vma=False
    )
```
